512 devices in a mesh: section: 8 (over z), dp: 64 (over x, y, core).
Axes of the slice: x: 4, y: 8, z: 8, core: 2. Of those that a mesh axis runs over, the one named last changes fastest.
Arguments:
- images: bfloat16 [128, 12, 12, 256], P('dp'), may hold values from -6 to 6
- dw_kernel: bfloat16 [8, 49, 256], P('section'), may hold values from -0.875 to 0.875
- ln_gain: bfloat16 [8, 256], P('section'), may hold values from 0.5 to 1.5
- w_in: bfloat16 [8, 256, 1024], P('section'), may hold values from -0.375 to 0.375
- w_out: bfloat16 [8, 1024, 256], P('section'), may hold values from -0.1875 to 0.1875
- layer_scale: bfloat16 [8, 256], P('section'), may hold values from 0.19921875 to 1
- scene_grad: bfloat16 [384, 12, 12, 256], P('dp'), may hold values from -6 to 6
- view_slot: int32 [128], P('dp'), may hold values from 0 to 383, as said below
Outputs:
- grad_kernel: bfloat16 [8, 49, 256], P('section')
- grad_gain: bfloat16 [8, 256], P('section')
- grad_in: bfloat16 [8, 256, 1024], P('section', None, 'dp')
- grad_out: bfloat16 [8, 1024, 256], P('section', 'dp')
- grad_scale: bfloat16 [8, 256], P('section')
The draws below stay inside these ranges and needn't reach their ends.
Inputs may be any that keep to these rules, and one draw needn't show every extreme that they name: `view_slot`: views v and w differ in slot unless v = w. Slot s is held by index s // 6 of dp; a view held by index d of dp has a slot held by d - 1, d or d + 1, and on holder o it is one of the slots (d - o + 1) * 2 to (d - o + 2) * 2 - 1 of that holder.
All inputs are finite; a program needn't handle non-finite values.
Results may differ from the reference program's by a relative error of at most 0.024.
Values may be sent and summed in bfloat16 or wider, within the bound.
No kernel may reach another device: no remote copies, remote signals or barrier semaphores. Data moves between devices by JAX's collectives and lax.ppermute only.
A program may use at most 64 MiB of HBM per device.

```python
import math
import jax
import jax.numpy as jnp
from jax import lax

C = 256
HID = 1024
KSIZE = 7
HH = 12
WW = 12
VIEW_DEV = 2
VIEWS = 128
SLOTS = 384
BLOCKS = 8
N_DP = 64


def draw_view_slot(key, part):
    group = VIEW_DEV
    slot_dev = 3 * VIEW_DEV

    def one_device(device_key, device):
        order = jax.random.permutation(device_key, 3 * group).astype(jnp.int32)
        candidate = jnp.arange(3 * group, dtype=jnp.int32)
        side = candidate // group
        owner = device - 1 + side
        valid = ((owner >= 0) & (owner < N_DP)).astype(jnp.int32)
        slot = owner * slot_dev + (2 - side) * group + candidate % group
        score = order + 3 * group * (1 - valid)
        picked = jnp.argsort(score, stable=True)[:VIEW_DEV]
        return slot[picked].astype(jnp.int32)
    keys = jax.random.split(jax.random.fold_in(key, 17), N_DP)
    devices = jnp.arange(N_DP, dtype=jnp.int32)
    return jax.vmap(one_device)(keys, devices).reshape(-1).astype(jnp.int32)


def levels(stream_key, dims, cuts, low, high):
    factor_of = 1.0
    for dim, shards_of in cuts:
        draws = jax.random.uniform(jax.random.fold_in(jax.random.fold_in(stream_key, 6), dim), (shards_of,), jnp.float32, low / len(cuts), high / len(cuts))
        factor_of = factor_of * jnp.repeat(jnp.exp(draws), dims[dim] // shards_of).reshape((-1,) + (1,) * (len(dims) - 1 - dim))
    return factor_of


def scatter_about(stream_key, shape, scale, reach, shards=(), kind=jnp.bfloat16):
    array = scale * jax.random.normal(stream_key, shape, jnp.float32)
    if shards:
        array = array * levels(stream_key, shape, shards, -0.22, 0.18)
    return jnp.clip(array, -reach, reach).astype(kind)


def setup_inputs(seed: int = 0) -> dict:
    key_of = jax.random.split(jax.random.key(seed), 9)
    return {
        "images": scatter_about(key_of[0], (VIEWS, HH, WW, C), 1.0, 6.0, ((0, 64),)),
        "dw_kernel": scatter_about(key_of[1], (BLOCKS, KSIZE * KSIZE, C), (KSIZE * KSIZE) ** -0.5, 0.875, ((0, 8),)),
        "ln_gain": jnp.clip(1.0 + 0.1 * jax.random.normal(key_of[2], (BLOCKS, C), jnp.float32), 0.5, 1.5).astype(jnp.bfloat16),
        "w_in": scatter_about(key_of[3], (BLOCKS, C, HID), C ** -0.5, 0.375, ((0, 8),)),
        "w_out": scatter_about(key_of[4], (BLOCKS, HID, C), HID ** -0.5, 0.1875, ((0, 8),)),
        "layer_scale": jnp.clip(jnp.exp(math.log(1.0) - 1.6133518 * jax.random.uniform(key_of[5], (BLOCKS, C), jnp.float32) ** levels(key_of[5], (BLOCKS, C), ((0, 8),), -0.2, 0.2)), 0.19921875, 1.0).astype(jnp.bfloat16),
        "scene_grad": scatter_about(key_of[6], (SLOTS, HH, WW, C), 1.0, 6.0, ((0, 64),)),
        "view_slot": draw_view_slot(jax.random.fold_in(key_of[8], 71), 0),
    }


ln_eps = 1e-06

def depthwise(inputs, kernel):
    height = inputs.shape[1]
    width = inputs.shape[2]
    margin = KSIZE // 2
    padded = jnp.pad(inputs, ((0, 0), (margin, margin), (margin, margin), (0, 0)))
    total = jnp.zeros(inputs.shape, jnp.float32)
    for row_tap in range(KSIZE):
        for col_tap in range(KSIZE):
            total = total + padded[:, row_tap:row_tap + height, col_tap:col_tap + width, :] * kernel[row_tap * KSIZE + col_tap]
    return total

def block_forward(inputs, params):
    kernel, norm_gain, proj_in, proj_out, scale = params
    channels = inputs.shape[-1]
    lead = inputs.shape[:-1]
    depthwise_output = depthwise(inputs.astype(jnp.float32), kernel)
    centered_input = lax.optimization_barrier(jnp.mean(depthwise_output, axis=-1, keepdims=True))
    spread = lax.optimization_barrier(jnp.mean((depthwise_output - centered_input) ** 2, axis=-1, keepdims=True))
    inverse_deviation = lax.rsqrt(spread + ln_eps)
    standardized_input = (depthwise_output - centered_input) * inverse_deviation
    normalized_input = (standardized_input * norm_gain).astype(jnp.bfloat16)
    channel_mixed = jnp.dot(normalized_input.reshape(-1, channels), proj_in, preferred_element_type=jnp.float32)
    hidden_expanded = jax.nn.gelu(channel_mixed, approximate=False).astype(jnp.bfloat16)
    residual_return = jnp.dot(hidden_expanded, proj_out, preferred_element_type=jnp.float32).reshape(lead + (channels,))
    block_output = (inputs.astype(jnp.float32) + scale * residual_return).astype(jnp.bfloat16)
    saved_residuals = (standardized_input, inverse_deviation, normalized_input, channel_mixed, hidden_expanded, residual_return)
    return (block_output, saved_residuals)

def block_backward(inputs, params, arrived):
    kernel, norm_gain, proj_in, proj_out, scale = params
    _, saved_residuals = block_forward(inputs, params)
    standardized_input, inverse_deviation, normalized_input, channel_mixed, hidden_expanded, residual_return = saved_residuals
    channels = inputs.shape[-1]
    height = inputs.shape[1]
    width = inputs.shape[2]
    lead = inputs.shape[:-1]
    incoming = arrived.astype(jnp.float32)
    g_scale = lax.optimization_barrier(jnp.sum(incoming * residual_return, axis=(0, 1, 2)))
    ct_back = (incoming * scale).astype(jnp.bfloat16).reshape(-1, channels)
    g_out = jnp.dot(hidden_expanded.T, ct_back, preferred_element_type=jnp.float32)
    ct_hidden = jnp.dot(ct_back, proj_out.T, preferred_element_type=jnp.float32).astype(jnp.bfloat16).astype(jnp.float32)
    slope = 0.5 * (1.0 + lax.erf(channel_mixed * (1.0 / math.sqrt(2.0)))) + channel_mixed * jnp.exp(-0.5 * channel_mixed * channel_mixed) * (1.0 / math.sqrt(2.0 * math.pi))
    ct_mixed = (ct_hidden * slope).astype(jnp.bfloat16)
    g_in = jnp.dot(normalized_input.reshape(-1, channels).T, ct_mixed, preferred_element_type=jnp.float32)
    normalized_cotangent = jnp.dot(ct_mixed, proj_in.T, preferred_element_type=jnp.float32).astype(jnp.bfloat16).astype(jnp.float32)
    normalized_cotangent = normalized_cotangent.reshape(lead + (channels,))
    norm_gain_gradient = lax.optimization_barrier(jnp.sum(normalized_cotangent * standardized_input, axis=(0, 1, 2)))
    standardized_cotangent = normalized_cotangent * norm_gain
    depthwise_cotangent = inverse_deviation * (standardized_cotangent - lax.optimization_barrier(jnp.mean(standardized_cotangent, axis=-1, keepdims=True)) - standardized_input * lax.optimization_barrier(jnp.mean(standardized_cotangent * standardized_input, axis=-1, keepdims=True)))
    margin = KSIZE // 2
    pad_spec = ((0, 0), (margin, margin), (margin, margin), (0, 0))
    padded_x = jnp.pad(inputs.astype(jnp.float32), pad_spec)
    padded_ct = jnp.pad(depthwise_cotangent, pad_spec)
    kernel_rows = []
    ct_inputs = incoming
    for row_tap in range(KSIZE):
        for col_tap in range(KSIZE):
            window = padded_x[:, row_tap:row_tap + height, col_tap:col_tap + width, :]
            kernel_rows.append(lax.optimization_barrier(jnp.sum(depthwise_cotangent * window, axis=(0, 1, 2))))
            flip_row = KSIZE - 1 - row_tap
            flip_col = KSIZE - 1 - col_tap
            ct_inputs = ct_inputs + padded_ct[:, flip_row:flip_row + height, flip_col:flip_col + width, :] * kernel[row_tap * KSIZE + col_tap]
    g_kernel = jnp.stack(kernel_rows, axis=0)
    return (ct_inputs.astype(jnp.bfloat16), (g_kernel, norm_gain_gradient, g_in, g_out, g_scale))

def reference(images, dw_kernel, ln_gain, w_in, w_out, layer_scale, scene_grad, view_slot):
    cotangent = jnp.take(scene_grad, view_slot.astype(jnp.int32), axis=0)
    groups_in = images.reshape(N_DP, VIEW_DEV, HH, WW, C)
    groups_ct = cotangent.reshape(N_DP, VIEW_DEV, HH, WW, C)

    def params_of(index):
        return (dw_kernel[index].astype(jnp.float32), ln_gain[index].astype(jnp.float32), w_in[index], w_out[index], layer_scale[index].astype(jnp.float32))

    def accumulate(totals, item):
        inputs, target = item
        stored = []
        value = inputs
        for index in range(BLOCKS):
            stored.append(value)
            value, _ = block_forward(value, params_of(index))
        arrived = target
        new_totals = list(totals)
        for index in reversed(range(BLOCKS)):
            arrived, terms = block_backward(stored[index], params_of(index), arrived)
            new_totals = [total.at[index].add(term) for total, term in zip(new_totals, terms)]
        return (tuple(new_totals), None)
    start = (jnp.zeros((BLOCKS, KSIZE * KSIZE, C), jnp.float32), jnp.zeros((BLOCKS, C), jnp.float32), jnp.zeros((BLOCKS, C, HID), jnp.float32), jnp.zeros((BLOCKS, HID, C), jnp.float32), jnp.zeros((BLOCKS, C), jnp.float32))
    totals, _ = lax.scan(accumulate, start, (groups_in, groups_ct))
    factor = 1.0 / math.sqrt(VIEWS * HH * WW)
    results = tuple(((member * factor).astype(jnp.bfloat16) for member in totals))
    return (results[0], results[1], results[2], results[3], results[4])
```

```python
import math

import jax
import jax.numpy as jnp
from jax import lax
from jax.sharding import PartitionSpec as P

ln_eps = 1e-06


def padded_2(block, sides, width):
    for axis, dim in sides:
        count = lax.axis_size(axis)
        forward = [(i, i + 1) for i in range(count - 1)]
        backward = [(target, source) for source, target in forward]
        low = lax.ppermute(
            lax.slice_in_dim(block, block.shape[dim] - width, None, axis=dim), axis, forward
        )
        high = lax.ppermute(lax.slice_in_dim(block, 0, width, axis=dim), axis, backward)
        block = jnp.concatenate([low, block, high], axis=dim)
    return block


def from_behind(block, axis, distance):
    devices = range(lax.axis_size(axis))
    route = [(i - distance, i) for i in devices if i - distance in devices]
    return lax.ppermute(block, axis, route)


def depthwise(inputs, kernel, ksize):
    height = inputs.shape[1]
    width = inputs.shape[2]
    margin = ksize // 2
    padded = jnp.pad(inputs, ((0, 0), (margin, margin), (margin, margin), (0, 0)))
    total = jnp.zeros(inputs.shape, jnp.float32)
    for row_tap in range(ksize):
        for col_tap in range(ksize):
            total = (
                total
                + padded[:, row_tap : row_tap + height, col_tap : col_tap + width, :]
                * kernel[row_tap * ksize + col_tap]
            )
    return total


def block_forward(inputs, params, ksize):
    kernel, norm_gain, proj_in, proj_out, scale = params
    channels = inputs.shape[-1]
    lead = inputs.shape[:-1]
    depthwise_output = depthwise(inputs.astype(jnp.float32), kernel, ksize)
    centered_input = jnp.mean(depthwise_output, axis=-1, keepdims=True)
    spread = jnp.mean((depthwise_output - centered_input) ** 2, axis=-1, keepdims=True)
    inverse_deviation = lax.rsqrt(spread + ln_eps)
    standardized_input = (depthwise_output - centered_input) * inverse_deviation
    normalized_input = (standardized_input * norm_gain).astype(jnp.bfloat16)
    channel_mixed = jnp.dot(
        normalized_input.reshape(-1, channels), proj_in, preferred_element_type=jnp.float32
    )
    hidden_expanded = jax.nn.gelu(channel_mixed, approximate=False).astype(jnp.bfloat16)
    residual_return = jnp.dot(
        hidden_expanded, proj_out, preferred_element_type=jnp.float32
    ).reshape(lead + (channels,))
    block_output = (inputs.astype(jnp.float32) + scale * residual_return).astype(jnp.bfloat16)
    return (
        block_output,
        (
            standardized_input,
            inverse_deviation,
            normalized_input,
            channel_mixed,
            hidden_expanded,
            residual_return,
        ),
    )


def block_backward(inputs, params, arrived, ksize, saved_residuals):
    kernel, norm_gain, proj_in, proj_out, scale = params
    (
        standardized_input,
        inverse_deviation,
        normalized_input,
        channel_mixed,
        hidden_expanded,
        residual_return,
    ) = saved_residuals
    channels = inputs.shape[-1]
    height = inputs.shape[1]
    width = inputs.shape[2]
    lead = inputs.shape[:-1]
    incoming = arrived.astype(jnp.float32)
    g_scale = jnp.sum(incoming * residual_return, axis=(0, 1, 2))
    ct_back = (incoming * scale).astype(jnp.bfloat16).reshape(-1, channels)
    g_out = jnp.dot(hidden_expanded.T, ct_back, preferred_element_type=jnp.float32)
    ct_hidden = (
        jnp.dot(ct_back, proj_out.T, preferred_element_type=jnp.float32)
        .astype(jnp.bfloat16)
        .astype(jnp.float32)
    )
    slope = 0.5 * (1.0 + lax.erf(channel_mixed * (1.0 / math.sqrt(2.0)))) + channel_mixed * jnp.exp(
        -0.5 * channel_mixed * channel_mixed
    ) * (1.0 / math.sqrt(2.0 * math.pi))
    ct_mixed = (ct_hidden * slope).astype(jnp.bfloat16)
    g_in = jnp.dot(
        normalized_input.reshape(-1, channels).T, ct_mixed, preferred_element_type=jnp.float32
    )
    normalized_cotangent = (
        jnp.dot(ct_mixed, proj_in.T, preferred_element_type=jnp.float32)
        .astype(jnp.bfloat16)
        .astype(jnp.float32)
    )
    normalized_cotangent = normalized_cotangent.reshape(lead + (channels,))
    norm_gain_gradient = jnp.sum(normalized_cotangent * standardized_input, axis=(0, 1, 2))
    standardized_cotangent = normalized_cotangent * norm_gain
    depthwise_cotangent = inverse_deviation * (
        standardized_cotangent
        - jnp.mean(standardized_cotangent, axis=-1, keepdims=True)
        - standardized_input
        * jnp.mean(standardized_cotangent * standardized_input, axis=-1, keepdims=True)
    )
    margin = ksize // 2
    pad_spec = ((0, 0), (margin, margin), (margin, margin), (0, 0))
    padded_x = jnp.pad(inputs.astype(jnp.float32), pad_spec)
    padded_ct = jnp.pad(depthwise_cotangent, pad_spec)
    kernel_rows = []
    ct_inputs = incoming
    for row_tap in range(ksize):
        for col_tap in range(ksize):
            window = padded_x[:, row_tap : row_tap + height, col_tap : col_tap + width, :]
            kernel_rows.append(jnp.sum(depthwise_cotangent * window, axis=(0, 1, 2)))
            flip_row = ksize - 1 - row_tap
            flip_col = ksize - 1 - col_tap
            ct_inputs = (
                ct_inputs
                + padded_ct[:, flip_row : flip_row + height, flip_col : flip_col + width, :]
                * kernel[row_tap * ksize + col_tap]
            )
    g_kernel = jnp.stack(kernel_rows, axis=0)
    return (ct_inputs.astype(jnp.bfloat16), (g_kernel, norm_gain_gradient, g_in, g_out, g_scale))


def dp_reduce(g_in, g_out, small, axis):
    holders = lax.axis_size(axis)
    bits = holders.bit_length() - 1
    assert 1 << bits == holders
    me = lax.axis_index(axis)
    channels, hidden = g_in.shape
    share = hidden // holders
    blocks_in = g_in.reshape(channels, holders, share).transpose(1, 0, 2).reshape(holders, -1)
    blocks_out = g_out.reshape(holders, share * channels)
    big = jnp.concatenate([blocks_in, blocks_out], axis=1)
    width = big.shape[1]
    big = big.reshape((2,) * bits + (width,))
    remaining = list(range(bits - 1, -1, -1))
    order = [0] + [b for b in (1, 4, 2, 5, 3) if b < bits] + [b for b in range(6, bits)]
    for bit in order:
        position = remaining.index(bit)
        mine = (me >> bit) & 1
        keep = lax.dynamic_index_in_dim(big, mine, position, keepdims=False)
        send = lax.dynamic_index_in_dim(big, 1 - mine, position, keepdims=False)
        shape = keep.shape
        packet = jnp.concatenate([send.reshape(-1), small])
        pairs = [(d, d ^ (1 << bit)) for d in range(holders)]
        got = lax.ppermute(packet, axis, pairs)
        big = keep + got[: keep.size].reshape(shape)
        small = small + got[keep.size :]
        remaining.pop(position)
    big = big.reshape(width)
    s_in = big[: channels * share].reshape(channels, share)
    s_out = big[channels * share :].reshape(share, channels)
    return s_in, s_out, small


def per_device(images, dw_kernel, ln_gain, w_in, w_out, layer_scale, scene_grad, view_slot):
    section_id = lax.axis_index("section")
    sections = lax.axis_size("section")
    holder_id = lax.axis_index("dp")
    holders = lax.axis_size("dp")
    views = images.shape[0]
    slot_dev = scene_grad.shape[0]
    ksize = math.isqrt(dw_kernel.shape[1])
    params = (
        dw_kernel[0].astype(jnp.float32),
        ln_gain[0].astype(jnp.float32),
        w_in[0],
        w_out[0],
        layer_scale[0].astype(jnp.float32),
    )
    holder = view_slot // slot_dev
    local_row = view_slot % slot_dev
    side = holder - holder_id + 1
    extended = padded_2(scene_grad, (("dp", 0),), slot_dev)
    rows = side * slot_dev + local_row
    targets = jnp.take(extended, rows, axis=0)
    ticks = views + sections - 1
    empty_map = jnp.zeros(images.shape[1:], jnp.bfloat16)

    def run_block(current):
        out, res = block_forward(current[None], params, ksize)
        return out[0], res

    probe = jax.eval_shape(run_block, empty_map)[1]
    start_store = (
        jnp.zeros((views + 1,) + images.shape[1:], images.dtype),
        jax.tree.map(lambda r: jnp.zeros((views + 1,) + r.shape, r.dtype), probe),
    )

    def forward_tick(tick, carry):
        incoming, store = carry
        micro = tick - section_id
        valid = (micro >= 0) & (micro < views)
        index = jnp.where(valid, micro, views)
        own_image = lax.dynamic_index_in_dim(
            images, jnp.clip(tick, 0, views - 1), 0, keepdims=False
        )
        current = jnp.where(section_id == 0, own_image, incoming)
        result, res = run_block(current)
        incoming = from_behind(result, "section", 1)
        store = jax.tree.map(
            lambda buf, val: lax.dynamic_update_index_in_dim(buf, val, index, 0),
            store,
            (current, res),
        )
        return (incoming, store)

    _, (saved_inputs, saved_res) = lax.fori_loop(
        0, ticks, forward_tick, (empty_map, start_store)
    )

    def backward_step(current, arrived, res):
        back_x, back_p = block_backward(current[None], params, arrived[None], ksize, res)
        return (back_x[0], back_p)

    start_totals = jax.tree.map(lambda member: jnp.zeros(member.shape, jnp.float32), params)

    def backward_tick(tick, carry):
        incoming, totals = carry
        micro = tick - (sections - 1 - section_id)
        valid = (micro >= 0) & (micro < views)
        index = jnp.clip(micro, 0, views - 1)
        own_target = lax.dynamic_index_in_dim(targets, index, 0, keepdims=False)
        arrived = jnp.where(section_id == sections - 1, own_target, incoming)
        current = lax.dynamic_index_in_dim(saved_inputs, index, 0, keepdims=False)
        res = jax.tree.map(
            lambda buf: lax.dynamic_index_in_dim(buf, index, 0, keepdims=False), saved_res
        )
        back_x, back_p = backward_step(current, arrived, res)
        totals = jax.tree.map(
            lambda total, term: total + jnp.where(valid, term, 0.0), totals, back_p
        )
        incoming = from_behind(back_x, "section", -1)
        return (incoming, totals)

    _, totals = lax.fori_loop(0, ticks, backward_tick, (empty_map, start_totals))
    g_kernel, norm_gain_gradient, g_in, g_out, g_scale = totals
    small = jnp.concatenate(
        [g_kernel.reshape(-1), norm_gain_gradient.reshape(-1), g_scale.reshape(-1)]
    )
    s_in, s_out, small = dp_reduce(g_in, g_out, small, "dp")
    n_kernel = g_kernel.size
    n_gain = norm_gain_gradient.size
    s_kernel = small[:n_kernel].reshape(g_kernel.shape)
    s_gain = small[n_kernel : n_kernel + n_gain].reshape(norm_gain_gradient.shape)
    s_scale = small[n_kernel + n_gain :].reshape(g_scale.shape)
    factor = 1.0 / math.sqrt(views * holders * images.shape[1] * images.shape[2])
    return (
        (s_kernel * factor).astype(jnp.bfloat16)[None],
        (s_gain * factor).astype(jnp.bfloat16)[None],
        (s_in * factor).astype(jnp.bfloat16)[None],
        (s_out * factor).astype(jnp.bfloat16)[None],
        (s_scale * factor).astype(jnp.bfloat16)[None],
    )


def solution(mesh):
    return jax.shard_map(
        per_device,
        mesh=mesh,
        in_specs=(
            P("dp", None, None, None),
            P("section", None, None),
            P("section", None),
            P("section", None, None),
            P("section", None, None),
            P("section", None),
            P("dp", None, None, None),
            P("dp"),
        ),
        out_specs=(
            P("section", None, None),
            P("section", None),
            P("section", None, "dp"),
            P("section", "dp", None),
            P("section", None),
        ),
        check_vma=False,
    )
```

```python
import math

import jax
import jax.numpy as jnp
from jax import lax
from jax.sharding import PartitionSpec as P

ln_eps = 1e-06


def padded_2(block, sides, width):
    for axis, dim in sides:
        count = lax.axis_size(axis)
        forward = [(i, i + 1) for i in range(count - 1)]
        backward = [(target, source) for source, target in forward]
        low = lax.ppermute(
            lax.slice_in_dim(block, block.shape[dim] - width, None, axis=dim), axis, forward
        )
        high = lax.ppermute(lax.slice_in_dim(block, 0, width, axis=dim), axis, backward)
        block = jnp.concatenate([low, block, high], axis=dim)
    return block


def from_behind(block, axis, distance):
    devices = range(lax.axis_size(axis))
    route = [(i - distance, i) for i in devices if i - distance in devices]
    return lax.ppermute(block, axis, route)


def depthwise(inputs, kernel, ksize):
    height = inputs.shape[1]
    width = inputs.shape[2]
    margin = ksize // 2
    padded = jnp.pad(inputs, ((0, 0), (margin, margin), (margin, margin), (0, 0)))
    total = jnp.zeros(inputs.shape, jnp.float32)
    for row_tap in range(ksize):
        for col_tap in range(ksize):
            total = (
                total
                + padded[:, row_tap : row_tap + height, col_tap : col_tap + width, :]
                * kernel[row_tap * ksize + col_tap]
            )
    return total


def block_forward(inputs, params, ksize):
    kernel, norm_gain, proj_in, proj_out, scale = params
    channels = inputs.shape[-1]
    lead = inputs.shape[:-1]
    depthwise_output = depthwise(inputs.astype(jnp.float32), kernel, ksize)
    centered_input = jnp.mean(depthwise_output, axis=-1, keepdims=True)
    spread = jnp.mean((depthwise_output - centered_input) ** 2, axis=-1, keepdims=True)
    inverse_deviation = lax.rsqrt(spread + ln_eps)
    standardized_input = (depthwise_output - centered_input) * inverse_deviation
    normalized_input = (standardized_input * norm_gain).astype(jnp.bfloat16)
    channel_mixed = jnp.dot(
        normalized_input.reshape(-1, channels), proj_in, preferred_element_type=jnp.float32
    )
    hidden_expanded = jax.nn.gelu(channel_mixed, approximate=False).astype(jnp.bfloat16)
    residual_return = jnp.dot(
        hidden_expanded, proj_out, preferred_element_type=jnp.float32
    ).reshape(lead + (channels,))
    block_output = (inputs.astype(jnp.float32) + scale * residual_return).astype(jnp.bfloat16)
    return (
        block_output,
        (
            standardized_input,
            inverse_deviation,
            normalized_input,
            channel_mixed,
            hidden_expanded,
            residual_return,
        ),
    )


def block_backward(inputs, params, arrived, ksize, saved_residuals):
    kernel, norm_gain, proj_in, proj_out, scale = params
    (
        standardized_input,
        inverse_deviation,
        normalized_input,
        channel_mixed,
        hidden_expanded,
        residual_return,
    ) = saved_residuals
    channels = inputs.shape[-1]
    height = inputs.shape[1]
    width = inputs.shape[2]
    lead = inputs.shape[:-1]
    incoming = arrived.astype(jnp.float32)
    g_scale = jnp.sum(incoming * residual_return, axis=(0, 1, 2))
    ct_back = (incoming * scale).astype(jnp.bfloat16).reshape(-1, channels)
    g_out = jnp.dot(hidden_expanded.T, ct_back, preferred_element_type=jnp.float32)
    ct_hidden = (
        jnp.dot(ct_back, proj_out.T, preferred_element_type=jnp.float32)
        .astype(jnp.bfloat16)
        .astype(jnp.float32)
    )
    slope = 0.5 * (1.0 + lax.erf(channel_mixed * (1.0 / math.sqrt(2.0)))) + channel_mixed * jnp.exp(
        -0.5 * channel_mixed * channel_mixed
    ) * (1.0 / math.sqrt(2.0 * math.pi))
    ct_mixed = (ct_hidden * slope).astype(jnp.bfloat16)
    g_in = jnp.dot(
        ct_mixed.T, normalized_input.reshape(-1, channels), preferred_element_type=jnp.float32
    )
    normalized_cotangent = (
        jnp.dot(ct_mixed, proj_in.T, preferred_element_type=jnp.float32)
        .astype(jnp.bfloat16)
        .astype(jnp.float32)
    )
    normalized_cotangent = normalized_cotangent.reshape(lead + (channels,))
    norm_gain_gradient = jnp.sum(normalized_cotangent * standardized_input, axis=(0, 1, 2))
    standardized_cotangent = normalized_cotangent * norm_gain
    depthwise_cotangent = inverse_deviation * (
        standardized_cotangent
        - jnp.mean(standardized_cotangent, axis=-1, keepdims=True)
        - standardized_input
        * jnp.mean(standardized_cotangent * standardized_input, axis=-1, keepdims=True)
    )
    margin = ksize // 2
    pad_spec = ((0, 0), (margin, margin), (margin, margin), (0, 0))
    padded_x = jnp.pad(inputs.astype(jnp.float32), pad_spec)
    padded_ct = jnp.pad(depthwise_cotangent, pad_spec)
    kernel_rows = []
    ct_inputs = incoming
    for row_tap in range(ksize):
        for col_tap in range(ksize):
            window = padded_x[:, row_tap : row_tap + height, col_tap : col_tap + width, :]
            kernel_rows.append(jnp.sum(depthwise_cotangent * window, axis=(0, 1, 2)))
            flip_row = ksize - 1 - row_tap
            flip_col = ksize - 1 - col_tap
            ct_inputs = (
                ct_inputs
                + padded_ct[:, flip_row : flip_row + height, flip_col : flip_col + width, :]
                * kernel[row_tap * ksize + col_tap]
            )
    g_kernel = jnp.stack(kernel_rows, axis=0)
    return (ct_inputs.astype(jnp.bfloat16), (g_kernel, norm_gain_gradient, g_in, g_out, g_scale))


def dp_reduce(g_in_t, g_out, small, axis):
    holders = lax.axis_size(axis)
    bits = holders.bit_length() - 1
    assert 1 << bits == holders
    me = lax.axis_index(axis)
    hidden, channels = g_out.shape
    share = hidden // holders
    big = jnp.stack([g_in_t, g_out]).reshape((2,) + (2,) * bits + (share * channels,))
    remaining = list(range(bits - 1, -1, -1))
    order = [0] + [b for b in (1, 4, 2, 5, 3) if b < bits] + [b for b in range(6, bits)]
    for bit in order:
        position = remaining.index(bit) + 1
        mine = (me >> bit) & 1
        keep = lax.dynamic_index_in_dim(big, mine, position, keepdims=False)
        send = lax.dynamic_index_in_dim(big, 1 - mine, position, keepdims=False)
        small = small.astype(jnp.bfloat16).astype(jnp.float32)
        packet = jnp.concatenate([send.reshape(-1), small]).astype(jnp.bfloat16)
        pairs = [(d, d ^ (1 << bit)) for d in range(holders)]
        got = lax.ppermute(packet, axis, pairs).astype(jnp.float32)
        big = keep + got[: keep.size].reshape(keep.shape)
        small = small + got[keep.size :]
        remaining.pop(position - 1)
    big = big.reshape(2, share, channels)
    return big[0].T, big[1], small


def per_device(images, dw_kernel, ln_gain, w_in, w_out, layer_scale, scene_grad, view_slot):
    section_id = lax.axis_index("section")
    sections = lax.axis_size("section")
    holder_id = lax.axis_index("dp")
    holders = lax.axis_size("dp")
    views = images.shape[0]
    slot_dev = scene_grad.shape[0]
    ksize = math.isqrt(dw_kernel.shape[1])
    params = (
        dw_kernel[0].astype(jnp.float32),
        ln_gain[0].astype(jnp.float32),
        w_in[0],
        w_out[0],
        layer_scale[0].astype(jnp.float32),
    )
    holder = view_slot // slot_dev
    local_row = view_slot % slot_dev
    side = holder - holder_id + 1
    extended = padded_2(scene_grad, (("dp", 0),), slot_dev)
    rows = side * slot_dev + local_row
    targets = jnp.take(extended, rows, axis=0)
    ticks = views + sections - 1
    empty_map = jnp.zeros(images.shape[1:], jnp.bfloat16)

    def run_block(current):
        out, res = block_forward(current[None], params, ksize)
        return out[0], res

    probe = jax.eval_shape(run_block, empty_map)[1]
    start_store = (
        jnp.zeros((views + 1,) + images.shape[1:], images.dtype),
        jax.tree.map(lambda r: jnp.zeros((views + 1,) + r.shape, r.dtype), probe),
    )

    def forward_tick(tick, carry):
        incoming, store = carry
        micro = tick - section_id
        valid = (micro >= 0) & (micro < views)
        index = jnp.where(valid, micro, views)
        own_image = lax.dynamic_index_in_dim(
            images, jnp.clip(tick, 0, views - 1), 0, keepdims=False
        )
        current = jnp.where(section_id == 0, own_image, incoming)
        result, res = run_block(current)
        incoming = from_behind(result, "section", 1)
        store = jax.tree.map(
            lambda buf, val: lax.dynamic_update_index_in_dim(buf, val, index, 0),
            store,
            (current, res),
        )
        return (incoming, store)

    _, (saved_inputs, saved_res) = lax.fori_loop(
        0, ticks, forward_tick, (empty_map, start_store)
    )

    def backward_step(current, arrived, res):
        back_x, back_p = block_backward(current[None], params, arrived[None], ksize, res)
        return (back_x[0], back_p)

    start_totals = jax.tree.map(lambda member: jnp.zeros(member.shape, jnp.float32), params)
    start_totals = start_totals[:2] + (start_totals[2].T,) + start_totals[3:]

    def backward_tick(tick, carry):
        incoming, totals = carry
        micro = tick - (sections - 1 - section_id)
        valid = (micro >= 0) & (micro < views)
        index = jnp.clip(micro, 0, views - 1)
        own_target = lax.dynamic_index_in_dim(targets, index, 0, keepdims=False)
        arrived = jnp.where(section_id == sections - 1, own_target, incoming)
        current = lax.dynamic_index_in_dim(saved_inputs, index, 0, keepdims=False)
        res = jax.tree.map(
            lambda buf: lax.dynamic_index_in_dim(buf, index, 0, keepdims=False), saved_res
        )
        back_x, back_p = backward_step(current, arrived, res)
        totals = jax.tree.map(
            lambda total, term: total + jnp.where(valid, term, 0.0), totals, back_p
        )
        incoming = from_behind(back_x, "section", -1)
        return (incoming, totals)

    _, totals = lax.fori_loop(0, ticks, backward_tick, (empty_map, start_totals))
    g_kernel, norm_gain_gradient, g_in, g_out, g_scale = totals
    small = jnp.concatenate(
        [g_kernel.reshape(-1), norm_gain_gradient.reshape(-1), g_scale.reshape(-1)]
    )
    s_in, s_out, small = dp_reduce(g_in, g_out, small, "dp")
    n_kernel = g_kernel.size
    n_gain = norm_gain_gradient.size
    s_kernel = small[:n_kernel].reshape(g_kernel.shape)
    s_gain = small[n_kernel : n_kernel + n_gain].reshape(norm_gain_gradient.shape)
    s_scale = small[n_kernel + n_gain :].reshape(g_scale.shape)
    factor = 1.0 / math.sqrt(views * holders * images.shape[1] * images.shape[2])
    return (
        (s_kernel * factor).astype(jnp.bfloat16)[None],
        (s_gain * factor).astype(jnp.bfloat16)[None],
        (s_in * factor).astype(jnp.bfloat16)[None],
        (s_out * factor).astype(jnp.bfloat16)[None],
        (s_scale * factor).astype(jnp.bfloat16)[None],
    )


def solution(mesh):
    return jax.shard_map(
        per_device,
        mesh=mesh,
        in_specs=(
            P("dp", None, None, None),
            P("section", None, None),
            P("section", None),
            P("section", None, None),
            P("section", None, None),
            P("section", None),
            P("dp", None, None, None),
            P("dp"),
        ),
        out_specs=(
            P("section", None, None),
            P("section", None),
            P("section", None, "dp"),
            P("section", "dp", None),
            P("section", None),
        ),
        check_vma=False,
    )
```

```python
import math

import jax
import jax.numpy as jnp
from jax import lax
from jax.sharding import PartitionSpec as P

ln_eps = 1e-06


def padded_2(block, sides, width):
    for axis, dim in sides:
        count = lax.axis_size(axis)
        forward = [(i, i + 1) for i in range(count - 1)]
        backward = [(target, source) for source, target in forward]
        low = lax.ppermute(
            lax.slice_in_dim(block, block.shape[dim] - width, None, axis=dim), axis, forward
        )
        high = lax.ppermute(lax.slice_in_dim(block, 0, width, axis=dim), axis, backward)
        block = jnp.concatenate([low, block, high], axis=dim)
    return block


def from_behind(block, axis, distance):
    devices = range(lax.axis_size(axis))
    route = [(i - distance, i) for i in devices if i - distance in devices]
    return lax.ppermute(block, axis, route)


def depthwise(inputs, kernel, ksize):
    height = inputs.shape[1]
    width = inputs.shape[2]
    margin = ksize // 2
    padded = jnp.pad(inputs, ((0, 0), (margin, margin), (margin, margin), (0, 0)))
    total = jnp.zeros(inputs.shape, jnp.float32)
    for row_tap in range(ksize):
        for col_tap in range(ksize):
            total = (
                total
                + padded[:, row_tap : row_tap + height, col_tap : col_tap + width, :]
                * kernel[row_tap * ksize + col_tap]
            )
    return total


def block_forward(inputs, params, ksize):
    kernel, norm_gain, proj_in, proj_out, scale = params
    channels = inputs.shape[-1]
    lead = inputs.shape[:-1]
    depthwise_output = depthwise(inputs.astype(jnp.float32), kernel, ksize)
    centered_input = jnp.mean(depthwise_output, axis=-1, keepdims=True)
    spread = jnp.mean((depthwise_output - centered_input) ** 2, axis=-1, keepdims=True)
    inverse_deviation = lax.rsqrt(spread + ln_eps)
    standardized_input = (depthwise_output - centered_input) * inverse_deviation
    normalized_input = (standardized_input * norm_gain).astype(jnp.bfloat16)
    channel_mixed = jnp.dot(
        normalized_input.reshape(-1, channels), proj_in, preferred_element_type=jnp.float32
    )
    hidden_expanded = jax.nn.gelu(channel_mixed, approximate=False).astype(jnp.bfloat16)
    residual_return = jnp.dot(
        hidden_expanded, proj_out, preferred_element_type=jnp.float32
    ).reshape(lead + (channels,))
    block_output = (inputs.astype(jnp.float32) + scale * residual_return).astype(jnp.bfloat16)
    return (
        block_output,
        (
            standardized_input,
            inverse_deviation,
            normalized_input,
            channel_mixed,
            hidden_expanded,
            residual_return,
        ),
    )


def block_backward(inputs, params, arrived, ksize, saved_residuals):
    kernel, norm_gain, proj_in, proj_out, scale = params
    (
        standardized_input,
        inverse_deviation,
        normalized_input,
        channel_mixed,
        hidden_expanded,
        residual_return,
    ) = saved_residuals
    channels = inputs.shape[-1]
    height = inputs.shape[1]
    width = inputs.shape[2]
    lead = inputs.shape[:-1]
    incoming = arrived.astype(jnp.float32)
    g_scale = jnp.sum(incoming * residual_return, axis=(0, 1, 2))
    ct_back = (incoming * scale).astype(jnp.bfloat16).reshape(-1, channels)
    g_out = jnp.dot(hidden_expanded.T, ct_back, preferred_element_type=jnp.float32)
    ct_hidden = (
        jnp.dot(ct_back, proj_out.T, preferred_element_type=jnp.float32)
        .astype(jnp.bfloat16)
        .astype(jnp.float32)
    )
    slope = 0.5 * (1.0 + lax.erf(channel_mixed * (1.0 / math.sqrt(2.0)))) + channel_mixed * jnp.exp(
        -0.5 * channel_mixed * channel_mixed
    ) * (1.0 / math.sqrt(2.0 * math.pi))
    ct_mixed = (ct_hidden * slope).astype(jnp.bfloat16)
    g_in = jnp.dot(
        ct_mixed.T, normalized_input.reshape(-1, channels), preferred_element_type=jnp.float32
    )
    normalized_cotangent = (
        jnp.dot(ct_mixed, proj_in.T, preferred_element_type=jnp.float32)
        .astype(jnp.bfloat16)
        .astype(jnp.float32)
    )
    normalized_cotangent = normalized_cotangent.reshape(lead + (channels,))
    norm_gain_gradient = jnp.sum(normalized_cotangent * standardized_input, axis=(0, 1, 2))
    standardized_cotangent = normalized_cotangent * norm_gain
    depthwise_cotangent = inverse_deviation * (
        standardized_cotangent
        - jnp.mean(standardized_cotangent, axis=-1, keepdims=True)
        - standardized_input
        * jnp.mean(standardized_cotangent * standardized_input, axis=-1, keepdims=True)
    )
    margin = ksize // 2
    pad_spec = ((0, 0), (margin, margin), (margin, margin), (0, 0))
    padded_x = jnp.pad(inputs.astype(jnp.float32), pad_spec)
    padded_ct = jnp.pad(depthwise_cotangent, pad_spec)
    kernel_rows = []
    ct_inputs = incoming
    for row_tap in range(ksize):
        for col_tap in range(ksize):
            window = padded_x[:, row_tap : row_tap + height, col_tap : col_tap + width, :]
            kernel_rows.append(jnp.sum(depthwise_cotangent * window, axis=(0, 1, 2)))
            flip_row = ksize - 1 - row_tap
            flip_col = ksize - 1 - col_tap
            ct_inputs = (
                ct_inputs
                + padded_ct[:, flip_row : flip_row + height, flip_col : flip_col + width, :]
                * kernel[row_tap * ksize + col_tap]
            )
    g_kernel = jnp.stack(kernel_rows, axis=0)
    return (ct_inputs.astype(jnp.bfloat16), (g_kernel, norm_gain_gradient, g_in, g_out, g_scale))


def dp_reduce(g_in_t, g_out, small, axis):
    holders = lax.axis_size(axis)
    bits = holders.bit_length() - 1
    assert 1 << bits == holders
    me = lax.axis_index(axis)
    hidden, channels = g_out.shape
    share = hidden // holders
    big = jnp.stack([g_in_t, g_out]).reshape((2,) + (2,) * bits + (share * channels,))
    remaining = list(range(bits - 1, -1, -1))
    order = [0] + [b for b in (1, 4, 2, 5, 3) if b < bits] + [b for b in range(6, bits)]
    for bit in order:
        position = remaining.index(bit) + 1
        mine = (me >> bit) & 1
        keep = lax.dynamic_index_in_dim(big, mine, position, keepdims=False)
        send = lax.dynamic_index_in_dim(big, 1 - mine, position, keepdims=False)
        small = small.astype(jnp.bfloat16).astype(jnp.float32)
        packet = jnp.concatenate([send.reshape(-1), small]).astype(jnp.bfloat16)
        pairs = [(d, d ^ (1 << bit)) for d in range(holders)]
        got = lax.ppermute(packet, axis, pairs).astype(jnp.float32)
        big = keep + got[: keep.size].reshape(keep.shape)
        small = small + got[keep.size :]
        remaining.pop(position - 1)
    big = big.reshape(2, share, channels)
    return big[0].T, big[1], small


def per_device(images, dw_kernel, ln_gain, w_in, w_out, layer_scale, scene_grad, view_slot):
    section_id = lax.axis_index("section")
    sections = lax.axis_size("section")
    holder_id = lax.axis_index("dp")
    holders = lax.axis_size("dp")
    views = images.shape[0]
    slot_dev = scene_grad.shape[0]
    ksize = math.isqrt(dw_kernel.shape[1])
    params = (
        dw_kernel[0].astype(jnp.float32),
        ln_gain[0].astype(jnp.float32),
        w_in[0],
        w_out[0],
        layer_scale[0].astype(jnp.float32),
    )
    holder = view_slot // slot_dev
    local_row = view_slot % slot_dev
    side = holder - holder_id + 1
    from_left = from_behind(scene_grad[2 * views : 3 * views], "dp", 1)
    from_right = from_behind(scene_grad[0:views], "dp", -1)
    candidates = jnp.concatenate([from_left, scene_grad[views : 2 * views], from_right])
    rows = side * views + local_row - (2 - side) * views
    targets = jnp.take(candidates, rows, axis=0)
    ticks = views + sections - 1
    empty_map = jnp.zeros(images.shape[1:], jnp.bfloat16)

    def run_block(current):
        out, res = block_forward(current[None], params, ksize)
        return out[0], res

    probe = jax.eval_shape(run_block, empty_map)[1]
    start_store = (
        jnp.zeros((views + 1,) + images.shape[1:], images.dtype),
        jax.tree.map(lambda r: jnp.zeros((views + 1,) + r.shape, r.dtype), probe),
    )

    def forward_tick(tick, carry):
        incoming, store = carry
        micro = tick - section_id
        valid = (micro >= 0) & (micro < views)
        index = jnp.where(valid, micro, views)
        own_image = lax.dynamic_index_in_dim(
            images, jnp.clip(tick, 0, views - 1), 0, keepdims=False
        )
        current = jnp.where(section_id == 0, own_image, incoming)
        result, res = run_block(current)
        incoming = from_behind(result, "section", 1)
        store = jax.tree.map(
            lambda buf, val: lax.dynamic_update_index_in_dim(buf, val, index, 0),
            store,
            (current, res),
        )
        return (incoming, store)

    carry = (empty_map, start_store)
    for tick in range(ticks):
        carry = forward_tick(tick, carry)
    _, (saved_inputs, saved_res) = carry

    def backward_step(current, arrived, res):
        back_x, back_p = block_backward(current[None], params, arrived[None], ksize, res)
        return (back_x[0], back_p)

    start_totals = jax.tree.map(lambda member: jnp.zeros(member.shape, jnp.float32), params)
    start_totals = start_totals[:2] + (start_totals[2].T,) + start_totals[3:]

    def backward_tick(tick, carry):
        incoming, totals = carry
        micro = tick - (sections - 1 - section_id)
        valid = (micro >= 0) & (micro < views)
        index = jnp.clip(micro, 0, views - 1)
        own_target = lax.dynamic_index_in_dim(targets, index, 0, keepdims=False)
        arrived = jnp.where(section_id == sections - 1, own_target, incoming)
        current = lax.dynamic_index_in_dim(saved_inputs, index, 0, keepdims=False)
        res = jax.tree.map(
            lambda buf: lax.dynamic_index_in_dim(buf, index, 0, keepdims=False), saved_res
        )
        back_x, back_p = backward_step(current, arrived, res)
        totals = jax.tree.map(
            lambda total, term: total + jnp.where(valid, term, 0.0), totals, back_p
        )
        incoming = from_behind(back_x, "section", -1)
        return (incoming, totals)

    carry = (empty_map, start_totals)
    for tick in range(ticks):
        carry = backward_tick(tick, carry)
    _, totals = carry
    g_kernel, norm_gain_gradient, g_in, g_out, g_scale = totals
    small = jnp.concatenate(
        [g_kernel.reshape(-1), norm_gain_gradient.reshape(-1), g_scale.reshape(-1)]
    )
    s_in, s_out, small = dp_reduce(g_in, g_out, small, "dp")
    n_kernel = g_kernel.size
    n_gain = norm_gain_gradient.size
    s_kernel = small[:n_kernel].reshape(g_kernel.shape)
    s_gain = small[n_kernel : n_kernel + n_gain].reshape(norm_gain_gradient.shape)
    s_scale = small[n_kernel + n_gain :].reshape(g_scale.shape)
    factor = 1.0 / math.sqrt(views * holders * images.shape[1] * images.shape[2])
    return (
        (s_kernel * factor).astype(jnp.bfloat16)[None],
        (s_gain * factor).astype(jnp.bfloat16)[None],
        (s_in * factor).astype(jnp.bfloat16)[None],
        (s_out * factor).astype(jnp.bfloat16)[None],
        (s_scale * factor).astype(jnp.bfloat16)[None],
    )


def solution(mesh):
    return jax.shard_map(
        per_device,
        mesh=mesh,
        in_specs=(
            P("dp", None, None, None),
            P("section", None, None),
            P("section", None),
            P("section", None, None),
            P("section", None, None),
            P("section", None),
            P("dp", None, None, None),
            P("dp"),
        ),
        out_specs=(
            P("section", None, None),
            P("section", None),
            P("section", None, "dp"),
            P("section", "dp", None),
            P("section", None),
        ),
        check_vma=False,
    )
```

```python
import math

import jax
import jax.numpy as jnp
from jax import lax
from jax.sharding import PartitionSpec as P

ln_eps = 1e-06


def padded_2(block, sides, width):
    for axis, dim in sides:
        count = lax.axis_size(axis)
        forward = [(i, i + 1) for i in range(count - 1)]
        backward = [(target, source) for source, target in forward]
        low = lax.ppermute(
            lax.slice_in_dim(block, block.shape[dim] - width, None, axis=dim), axis, forward
        )
        high = lax.ppermute(lax.slice_in_dim(block, 0, width, axis=dim), axis, backward)
        block = jnp.concatenate([low, block, high], axis=dim)
    return block


def from_behind(block, axis, distance):
    devices = range(lax.axis_size(axis))
    route = [(i - distance, i) for i in devices if i - distance in devices]
    return lax.ppermute(block, axis, route)


def depthwise(inputs, kernel, ksize):
    height = inputs.shape[1]
    width = inputs.shape[2]
    margin = ksize // 2
    padded = jnp.pad(inputs, ((0, 0), (margin, margin), (margin, margin), (0, 0)))
    total = jnp.zeros(inputs.shape, jnp.float32)
    for row_tap in range(ksize):
        for col_tap in range(ksize):
            total = (
                total
                + padded[:, row_tap : row_tap + height, col_tap : col_tap + width, :]
                * kernel[row_tap * ksize + col_tap]
            )
    return total


def block_forward(inputs, params, ksize):
    kernel, norm_gain, proj_in, proj_out, scale = params
    channels = inputs.shape[-1]
    lead = inputs.shape[:-1]
    depthwise_output = depthwise(inputs.astype(jnp.float32), kernel, ksize)
    centered_input = jnp.mean(depthwise_output, axis=-1, keepdims=True)
    spread = jnp.mean((depthwise_output - centered_input) ** 2, axis=-1, keepdims=True)
    inverse_deviation = lax.rsqrt(spread + ln_eps)
    standardized_input = (depthwise_output - centered_input) * inverse_deviation
    normalized_input = (standardized_input * norm_gain).astype(jnp.bfloat16)
    channel_mixed = jnp.dot(
        normalized_input.reshape(-1, channels), proj_in, preferred_element_type=jnp.float32
    )
    hidden_expanded = jax.nn.gelu(channel_mixed, approximate=False).astype(jnp.bfloat16)
    slope = 0.5 * (1.0 + lax.erf(channel_mixed * (1.0 / math.sqrt(2.0)))) + channel_mixed * jnp.exp(
        -0.5 * channel_mixed * channel_mixed
    ) * (1.0 / math.sqrt(2.0 * math.pi))
    residual_return = jnp.dot(
        hidden_expanded, proj_out, preferred_element_type=jnp.float32
    ).reshape(lead + (channels,))
    block_output = (inputs.astype(jnp.float32) + scale * residual_return).astype(jnp.bfloat16)
    return (
        block_output,
        (
            standardized_input,
            inverse_deviation,
            normalized_input,
            slope,
            hidden_expanded,
            residual_return,
        ),
    )


def block_backward(inputs, params, arrived, ksize, saved_residuals):
    kernel, norm_gain, proj_in, proj_out, scale = params
    (
        standardized_input,
        inverse_deviation,
        normalized_input,
        slope,
        hidden_expanded,
        residual_return,
    ) = saved_residuals
    channels = inputs.shape[-1]
    height = inputs.shape[1]
    width = inputs.shape[2]
    lead = inputs.shape[:-1]
    incoming = arrived.astype(jnp.float32)
    g_scale = jnp.sum(incoming * residual_return, axis=(0, 1, 2))
    ct_back = (incoming * scale).astype(jnp.bfloat16).reshape(-1, channels)
    g_out = jnp.dot(hidden_expanded.T, ct_back, preferred_element_type=jnp.float32)
    ct_hidden = (
        jnp.dot(ct_back, proj_out.T, preferred_element_type=jnp.float32)
        .astype(jnp.bfloat16)
        .astype(jnp.float32)
    )
    ct_mixed = (ct_hidden * slope).astype(jnp.bfloat16)
    g_in = jnp.dot(
        ct_mixed.T, normalized_input.reshape(-1, channels), preferred_element_type=jnp.float32
    )
    normalized_cotangent = (
        jnp.dot(ct_mixed, proj_in.T, preferred_element_type=jnp.float32)
        .astype(jnp.bfloat16)
        .astype(jnp.float32)
    )
    normalized_cotangent = normalized_cotangent.reshape(lead + (channels,))
    norm_gain_gradient = jnp.sum(normalized_cotangent * standardized_input, axis=(0, 1, 2))
    standardized_cotangent = normalized_cotangent * norm_gain
    depthwise_cotangent = inverse_deviation * (
        standardized_cotangent
        - jnp.mean(standardized_cotangent, axis=-1, keepdims=True)
        - standardized_input
        * jnp.mean(standardized_cotangent * standardized_input, axis=-1, keepdims=True)
    )
    margin = ksize // 2
    pad_spec = ((0, 0), (margin, margin), (margin, margin), (0, 0))
    padded_x = jnp.pad(inputs.astype(jnp.float32), pad_spec)
    padded_ct = jnp.pad(depthwise_cotangent, pad_spec)
    kernel_rows = []
    ct_inputs = incoming
    for row_tap in range(ksize):
        for col_tap in range(ksize):
            window = padded_x[:, row_tap : row_tap + height, col_tap : col_tap + width, :]
            kernel_rows.append(jnp.sum(depthwise_cotangent * window, axis=(0, 1, 2)))
            flip_row = ksize - 1 - row_tap
            flip_col = ksize - 1 - col_tap
            ct_inputs = (
                ct_inputs
                + padded_ct[:, flip_row : flip_row + height, flip_col : flip_col + width, :]
                * kernel[row_tap * ksize + col_tap]
            )
    g_kernel = jnp.stack(kernel_rows, axis=0)
    return (ct_inputs.astype(jnp.bfloat16), (g_kernel, norm_gain_gradient, g_in, g_out, g_scale))


def dp_reduce(g_in_t, g_out, small, axis):
    holders = lax.axis_size(axis)
    bits = holders.bit_length() - 1
    assert 1 << bits == holders
    me = lax.axis_index(axis)
    hidden, channels = g_out.shape
    share = hidden // holders
    big = jnp.stack([g_in_t, g_out]).reshape((2,) + (2,) * bits + (share * channels,))
    remaining = list(range(bits - 1, -1, -1))
    order = [0] + [b for b in (1, 4, 2, 5, 3) if b < bits] + [b for b in range(6, bits)]
    for bit in order:
        position = remaining.index(bit) + 1
        mine = (me >> bit) & 1
        keep = lax.dynamic_index_in_dim(big, mine, position, keepdims=False)
        send = lax.dynamic_index_in_dim(big, 1 - mine, position, keepdims=False)
        small = small.astype(jnp.bfloat16).astype(jnp.float32)
        packet = jnp.concatenate([send.reshape(-1), small]).astype(jnp.bfloat16)
        pairs = [(d, d ^ (1 << bit)) for d in range(holders)]
        got = lax.ppermute(packet, axis, pairs).astype(jnp.float32)
        big = keep + got[: keep.size].reshape(keep.shape)
        small = small + got[keep.size :]
        remaining.pop(position - 1)
    big = big.reshape(2, share, channels)
    return big[0].T, big[1], small


def per_device(images, dw_kernel, ln_gain, w_in, w_out, layer_scale, scene_grad, view_slot):
    section_id = lax.axis_index("section")
    sections = lax.axis_size("section")
    holder_id = lax.axis_index("dp")
    holders = lax.axis_size("dp")
    views = images.shape[0]
    slot_dev = scene_grad.shape[0]
    ksize = math.isqrt(dw_kernel.shape[1])
    params = (
        dw_kernel[0].astype(jnp.float32),
        ln_gain[0].astype(jnp.float32),
        w_in[0],
        w_out[0],
        layer_scale[0].astype(jnp.float32),
    )
    holder = view_slot // slot_dev
    local_row = view_slot % slot_dev
    side = holder - holder_id + 1
    from_left = from_behind(scene_grad[2 * views : 3 * views], "dp", 1)
    from_right = from_behind(scene_grad[0:views], "dp", -1)
    candidates = jnp.concatenate([from_left, scene_grad[views : 2 * views], from_right])
    rows = side * views + local_row - (2 - side) * views
    targets = jnp.take(candidates, rows, axis=0)
    ticks = views + sections - 1
    empty_map = jnp.zeros(images.shape[1:], jnp.bfloat16)

    def run_block(current):
        out, res = block_forward(current[None], params, ksize)
        return out[0], res

    probe = jax.eval_shape(run_block, empty_map)[1]
    start_store = (
        jnp.zeros((views + 1,) + images.shape[1:], images.dtype),
        jax.tree.map(lambda r: jnp.zeros((views + 1,) + r.shape, r.dtype), probe),
    )

    def forward_tick(tick, carry):
        incoming, store = carry
        micro = tick - section_id
        valid = (micro >= 0) & (micro < views)
        index = jnp.where(valid, micro, views)
        own_image = lax.dynamic_index_in_dim(
            images, jnp.clip(tick, 0, views - 1), 0, keepdims=False
        )
        current = jnp.where(section_id == 0, own_image, incoming)
        result, res = run_block(current)
        incoming = from_behind(result, "section", 1)
        store = jax.tree.map(
            lambda buf, val: lax.dynamic_update_index_in_dim(buf, val, index, 0),
            store,
            (current, res),
        )
        return (incoming, store)

    _, (saved_inputs, saved_res) = lax.fori_loop(
        0, ticks, forward_tick, (empty_map, start_store)
    )

    def backward_step(current, arrived, res):
        back_x, back_p = block_backward(current[None], params, arrived[None], ksize, res)
        return (back_x[0], back_p)

    start_totals = jax.tree.map(lambda member: jnp.zeros(member.shape, jnp.float32), params)
    start_totals = start_totals[:2] + (start_totals[2].T,) + start_totals[3:]

    def backward_tick(tick, carry):
        incoming, totals = carry
        micro = tick - (sections - 1 - section_id)
        valid = (micro >= 0) & (micro < views)
        index = jnp.clip(micro, 0, views - 1)
        own_target = lax.dynamic_index_in_dim(targets, index, 0, keepdims=False)
        arrived = jnp.where(section_id == sections - 1, own_target, incoming)
        current = lax.dynamic_index_in_dim(saved_inputs, index, 0, keepdims=False)
        res = jax.tree.map(
            lambda buf: lax.dynamic_index_in_dim(buf, index, 0, keepdims=False), saved_res
        )
        back_x, back_p = backward_step(current, arrived, res)
        totals = jax.tree.map(
            lambda total, term: total + jnp.where(valid, term, 0.0), totals, back_p
        )
        incoming = from_behind(back_x, "section", -1)
        return (incoming, totals)

    _, totals = lax.fori_loop(0, ticks, backward_tick, (empty_map, start_totals))
    g_kernel, norm_gain_gradient, g_in, g_out, g_scale = totals
    small = jnp.concatenate(
        [g_kernel.reshape(-1), norm_gain_gradient.reshape(-1), g_scale.reshape(-1)]
    )
    s_in, s_out, small = dp_reduce(g_in, g_out, small, "dp")
    n_kernel = g_kernel.size
    n_gain = norm_gain_gradient.size
    s_kernel = small[:n_kernel].reshape(g_kernel.shape)
    s_gain = small[n_kernel : n_kernel + n_gain].reshape(norm_gain_gradient.shape)
    s_scale = small[n_kernel + n_gain :].reshape(g_scale.shape)
    factor = 1.0 / math.sqrt(views * holders * images.shape[1] * images.shape[2])
    return (
        (s_kernel * factor).astype(jnp.bfloat16)[None],
        (s_gain * factor).astype(jnp.bfloat16)[None],
        (s_in * factor).astype(jnp.bfloat16)[None],
        (s_out * factor).astype(jnp.bfloat16)[None],
        (s_scale * factor).astype(jnp.bfloat16)[None],
    )


def solution(mesh):
    return jax.shard_map(
        per_device,
        mesh=mesh,
        in_specs=(
            P("dp", None, None, None),
            P("section", None, None),
            P("section", None),
            P("section", None, None),
            P("section", None, None),
            P("section", None),
            P("dp", None, None, None),
            P("dp"),
        ),
        out_specs=(
            P("section", None, None),
            P("section", None),
            P("section", None, "dp"),
            P("section", "dp", None),
            P("section", None),
        ),
        check_vma=False,
    )
```

```python
import math

import jax
import jax.numpy as jnp
from jax import lax
from jax.sharding import PartitionSpec as P

ln_eps = 1e-06


def padded_2(block, sides, width):
    for axis, dim in sides:
        count = lax.axis_size(axis)
        forward = [(i, i + 1) for i in range(count - 1)]
        backward = [(target, source) for source, target in forward]
        low = lax.ppermute(
            lax.slice_in_dim(block, block.shape[dim] - width, None, axis=dim), axis, forward
        )
        high = lax.ppermute(lax.slice_in_dim(block, 0, width, axis=dim), axis, backward)
        block = jnp.concatenate([low, block, high], axis=dim)
    return block


def from_behind(block, axis, distance):
    devices = range(lax.axis_size(axis))
    route = [(i - distance, i) for i in devices if i - distance in devices]
    return lax.ppermute(block, axis, route)


def depthwise(inputs, kernel, ksize):
    height = inputs.shape[1]
    width = inputs.shape[2]
    margin = ksize // 2
    padded = jnp.pad(inputs, ((0, 0), (margin, margin), (margin, margin), (0, 0)))
    total = jnp.zeros(inputs.shape, jnp.float32)
    for row_tap in range(ksize):
        for col_tap in range(ksize):
            total = (
                total
                + padded[:, row_tap : row_tap + height, col_tap : col_tap + width, :]
                * kernel[row_tap * ksize + col_tap]
            )
    return total


def block_forward(inputs, params, ksize):
    kernel, norm_gain, proj_in, proj_out, scale = params
    channels = inputs.shape[-1]
    lead = inputs.shape[:-1]
    depthwise_output = depthwise(inputs.astype(jnp.float32), kernel, ksize)
    centered_input = jnp.mean(depthwise_output, axis=-1, keepdims=True)
    spread = jnp.mean((depthwise_output - centered_input) ** 2, axis=-1, keepdims=True)
    inverse_deviation = lax.rsqrt(spread + ln_eps)
    standardized_input = (depthwise_output - centered_input) * inverse_deviation
    normalized_input = (standardized_input * norm_gain).astype(jnp.bfloat16)
    channel_mixed = jnp.dot(
        normalized_input.reshape(-1, channels), proj_in, preferred_element_type=jnp.float32
    )
    hidden_expanded = jax.nn.gelu(channel_mixed, approximate=False).astype(jnp.bfloat16)
    residual_return = jnp.dot(
        hidden_expanded, proj_out, preferred_element_type=jnp.float32
    ).reshape(lead + (channels,))
    block_output = (inputs.astype(jnp.float32) + scale * residual_return).astype(jnp.bfloat16)
    return (
        block_output,
        (
            standardized_input,
            inverse_deviation,
            normalized_input,
            channel_mixed,
            hidden_expanded,
            residual_return,
        ),
    )


def block_backward(inputs, params, arrived, ksize, saved_residuals):
    kernel, norm_gain, proj_in, proj_out, scale = params
    (
        standardized_input,
        inverse_deviation,
        normalized_input,
        channel_mixed,
        hidden_expanded,
        residual_return,
    ) = saved_residuals
    channels = inputs.shape[-1]
    height = inputs.shape[1]
    width = inputs.shape[2]
    lead = inputs.shape[:-1]
    incoming = arrived.astype(jnp.float32)
    g_scale = jnp.sum(incoming * residual_return, axis=(0, 1, 2))
    ct_back = (incoming * scale).astype(jnp.bfloat16).reshape(-1, channels)
    g_out = jnp.dot(hidden_expanded.T, ct_back, preferred_element_type=jnp.float32)
    ct_hidden = (
        jnp.dot(ct_back, proj_out.T, preferred_element_type=jnp.float32)
        .astype(jnp.bfloat16)
        .astype(jnp.float32)
    )
    slope = 0.5 * (1.0 + lax.erf(channel_mixed * (1.0 / math.sqrt(2.0)))) + channel_mixed * jnp.exp(
        -0.5 * channel_mixed * channel_mixed
    ) * (1.0 / math.sqrt(2.0 * math.pi))
    ct_mixed = (ct_hidden * slope).astype(jnp.bfloat16)
    g_in = jnp.dot(
        ct_mixed.T, normalized_input.reshape(-1, channels), preferred_element_type=jnp.float32
    )
    normalized_cotangent = (
        jnp.dot(ct_mixed, proj_in.T, preferred_element_type=jnp.float32)
        .astype(jnp.bfloat16)
        .astype(jnp.float32)
    )
    normalized_cotangent = normalized_cotangent.reshape(lead + (channels,))
    norm_gain_gradient = jnp.sum(normalized_cotangent * standardized_input, axis=(0, 1, 2))
    standardized_cotangent = normalized_cotangent * norm_gain
    depthwise_cotangent = inverse_deviation * (
        standardized_cotangent
        - jnp.mean(standardized_cotangent, axis=-1, keepdims=True)
        - standardized_input
        * jnp.mean(standardized_cotangent * standardized_input, axis=-1, keepdims=True)
    )
    margin = ksize // 2
    pad_spec = ((0, 0), (margin, margin), (margin, margin), (0, 0))
    padded_x = jnp.pad(inputs.astype(jnp.float32), pad_spec)
    padded_ct = jnp.pad(depthwise_cotangent, pad_spec)
    kernel_rows = []
    ct_inputs = incoming
    for row_tap in range(ksize):
        for col_tap in range(ksize):
            window = padded_x[:, row_tap : row_tap + height, col_tap : col_tap + width, :]
            kernel_rows.append(jnp.sum(depthwise_cotangent * window, axis=(0, 1, 2)))
            flip_row = ksize - 1 - row_tap
            flip_col = ksize - 1 - col_tap
            ct_inputs = (
                ct_inputs
                + padded_ct[:, flip_row : flip_row + height, flip_col : flip_col + width, :]
                * kernel[row_tap * ksize + col_tap]
            )
    g_kernel = jnp.stack(kernel_rows, axis=0)
    return (ct_inputs.astype(jnp.bfloat16), (g_kernel, norm_gain_gradient, g_in, g_out, g_scale))


def dp_reduce(g_in_t, g_out, small, axis):
    holders = lax.axis_size(axis)
    bits = holders.bit_length() - 1
    assert 1 << bits == holders
    me = lax.axis_index(axis)
    hidden, channels = g_out.shape
    share = hidden // holders
    big = jnp.stack([g_in_t, g_out]).reshape((2,) + (2,) * bits + (share * channels,))
    remaining = list(range(bits - 1, -1, -1))
    order = [0] + [b for b in (1, 4, 2, 5, 3) if b < bits] + [b for b in range(6, bits)]
    groups = [order[i : i + 2] for i in range(0, len(order), 2)]
    for group in groups:
        positions = [remaining.index(b) + 1 for b in group]
        mine = [(me >> b) & 1 for b in group]

        def chunk(values, big=big, positions=positions):
            part = big
            for p, v in sorted(zip(positions, values), key=lambda t: -t[0]):
                part = lax.dynamic_index_in_dim(part, v, p, keepdims=False)
            return part

        keep = chunk(mine)
        small = small.astype(jnp.bfloat16).astype(jnp.float32)
        received = [None]
        for code in range(1, 1 << len(group)):
            flips = [(code >> j) & 1 for j in range(len(group))]
            send = chunk([m ^ f for m, f in zip(mine, flips)])
            packet = jnp.concatenate([send.reshape(-1), small]).astype(jnp.bfloat16)
            mask = sum(f << b for f, b in zip(flips, group))
            pairs = [(d, d ^ mask) for d in range(holders)]
            received.append(lax.ppermute(packet, axis, pairs).astype(jnp.float32))
        big = keep
        for got in received[1:]:
            big = big + got[: keep.size].reshape(keep.shape)
        stacked = jnp.stack([small] + [got[keep.size :] for got in received[1:]])
        my_code = sum(m << j for j, m in enumerate(mine))
        terms = [
            lax.dynamic_index_in_dim(stacked, my_code ^ a, 0, keepdims=False)
            for a in range(1 << len(group))
        ]
        while len(terms) > 1:
            terms = [terms[i] + terms[i + 1] for i in range(0, len(terms), 2)]
        small = terms[0]
        for b in group:
            remaining.remove(b)
    big = big.reshape(2, share, channels)
    return big[0].T, big[1], small


def per_device(images, dw_kernel, ln_gain, w_in, w_out, layer_scale, scene_grad, view_slot):
    section_id = lax.axis_index("section")
    sections = lax.axis_size("section")
    holder_id = lax.axis_index("dp")
    holders = lax.axis_size("dp")
    views = images.shape[0]
    slot_dev = scene_grad.shape[0]
    ksize = math.isqrt(dw_kernel.shape[1])
    params = (
        dw_kernel[0].astype(jnp.float32),
        ln_gain[0].astype(jnp.float32),
        w_in[0],
        w_out[0],
        layer_scale[0].astype(jnp.float32),
    )
    holder = view_slot // slot_dev
    local_row = view_slot % slot_dev
    side = holder - holder_id + 1
    extended = padded_2(scene_grad, (("dp", 0),), slot_dev)
    rows = side * slot_dev + local_row
    targets = jnp.take(extended, rows, axis=0)
    ticks = views + sections - 1
    empty_map = jnp.zeros(images.shape[1:], jnp.bfloat16)

    def run_block(current):
        out, res = block_forward(current[None], params, ksize)
        return out[0], res

    probe = jax.eval_shape(run_block, empty_map)[1]
    start_store = (
        jnp.zeros((views + 1,) + images.shape[1:], images.dtype),
        jax.tree.map(lambda r: jnp.zeros((views + 1,) + r.shape, r.dtype), probe),
    )

    def forward_tick(tick, carry):
        incoming, store = carry
        micro = tick - section_id
        valid = (micro >= 0) & (micro < views)
        index = jnp.where(valid, micro, views)
        own_image = lax.dynamic_index_in_dim(
            images, jnp.clip(tick, 0, views - 1), 0, keepdims=False
        )
        current = jnp.where(section_id == 0, own_image, incoming)
        result, res = run_block(current)
        incoming = from_behind(result, "section", 1)
        store = jax.tree.map(
            lambda buf, val: lax.dynamic_update_index_in_dim(buf, val, index, 0),
            store,
            (current, res),
        )
        return (incoming, store)

    _, (saved_inputs, saved_res) = lax.fori_loop(
        0, ticks, forward_tick, (empty_map, start_store)
    )

    def backward_step(current, arrived, res):
        back_x, back_p = block_backward(current[None], params, arrived[None], ksize, res)
        return (back_x[0], back_p)

    start_totals = jax.tree.map(lambda member: jnp.zeros(member.shape, jnp.float32), params)
    start_totals = start_totals[:2] + (start_totals[2].T,) + start_totals[3:]

    def backward_tick(tick, carry):
        incoming, totals = carry
        micro = tick - (sections - 1 - section_id)
        valid = (micro >= 0) & (micro < views)
        index = jnp.clip(micro, 0, views - 1)
        own_target = lax.dynamic_index_in_dim(targets, index, 0, keepdims=False)
        arrived = jnp.where(section_id == sections - 1, own_target, incoming)
        current = lax.dynamic_index_in_dim(saved_inputs, index, 0, keepdims=False)
        res = jax.tree.map(
            lambda buf: lax.dynamic_index_in_dim(buf, index, 0, keepdims=False), saved_res
        )
        back_x, back_p = backward_step(current, arrived, res)
        totals = jax.tree.map(
            lambda total, term: total + jnp.where(valid, term, 0.0), totals, back_p
        )
        incoming = from_behind(back_x, "section", -1)
        return (incoming, totals)

    _, totals = lax.fori_loop(0, ticks, backward_tick, (empty_map, start_totals))
    g_kernel, norm_gain_gradient, g_in, g_out, g_scale = totals
    small = jnp.concatenate(
        [g_kernel.reshape(-1), norm_gain_gradient.reshape(-1), g_scale.reshape(-1)]
    )
    s_in, s_out, small = dp_reduce(g_in, g_out, small, "dp")
    n_kernel = g_kernel.size
    n_gain = norm_gain_gradient.size
    s_kernel = small[:n_kernel].reshape(g_kernel.shape)
    s_gain = small[n_kernel : n_kernel + n_gain].reshape(norm_gain_gradient.shape)
    s_scale = small[n_kernel + n_gain :].reshape(g_scale.shape)
    factor = 1.0 / math.sqrt(views * holders * images.shape[1] * images.shape[2])
    return (
        (s_kernel * factor).astype(jnp.bfloat16)[None],
        (s_gain * factor).astype(jnp.bfloat16)[None],
        (s_in * factor).astype(jnp.bfloat16)[None],
        (s_out * factor).astype(jnp.bfloat16)[None],
        (s_scale * factor).astype(jnp.bfloat16)[None],
    )


def solution(mesh):
    return jax.shard_map(
        per_device,
        mesh=mesh,
        in_specs=(
            P("dp", None, None, None),
            P("section", None, None),
            P("section", None),
            P("section", None, None),
            P("section", None, None),
            P("section", None),
            P("dp", None, None, None),
            P("dp"),
        ),
        out_specs=(
            P("section", None, None),
            P("section", None),
            P("section", None, "dp"),
            P("section", "dp", None),
            P("section", None),
        ),
        check_vma=False,
    )
```
